256 devices in a mesh: dp: 16 (over z, core), tensor: 16 (over y, x).
Axes of the slice: x: 4, y: 4, z: 8, core: 2. Of those that a mesh axis runs over, the one named last changes fastest.
Arguments:
- tokens: bfloat16 [2048, 8192], P(('dp', 'tensor')), may hold values from -6 to 6
- hidden_grad: bfloat16 [2048, 14336], P('dp', 'tensor'), may hold values from -1.5 to 1.5
- gate_tiles: bfloat16 [16, 208, 128, 128], P('tensor', 'dp'), may hold values from -0.125 to 0.125
- up_tiles: bfloat16 [16, 208, 128, 128], P('tensor', 'dp'), may hold values from -0.125 to 0.125
- tile_rows: int32 [2, 112, 16], P(None, 'tensor'), may hold values from 0 to 63, all different within a row
- tile_owner: int32 [2, 112, 16], P(None, 'tensor'), may hold values from 0 to 15, as said below
Outputs:
- hidden: bfloat16 [2048, 14336], P('dp', 'tensor')
- token_grad: bfloat16 [2048, 8192], P(('dp', 'tensor'))
- gate_grad: bfloat16 [16, 208, 128, 128], P('tensor', 'dp')
- up_grad: bfloat16 [16, 208, 128, 128], P('tensor', 'dp')
The draws below stay inside these ranges and needn't reach their ends.
Inputs may be any that keep to these rules, and one draw needn't show every extreme that they name: Each row tile_rows[m, f, :] names 16 different row blocks. For each m and t, among the 112 entries tile_owner[m, t * 7 .. (t + 1) * 7 - 1, :] no owner appears more than 13 times, and some owner appears exactly 13 times.
All inputs are finite; a program needn't handle non-finite values.
Results may differ from the reference program's by a relative error of at most 0.018.
Values may be sent and summed in bfloat16 or wider, within the bound.
No kernel may reach another device: no remote copies, remote signals or barrier semaphores. Data moves between devices by JAX's collectives and lax.ppermute only.
A program may use at most 128 MiB of HBM per device.

```python
import jax
import jax.numpy as jnp
from jax import lax

D = 8192
FF = 14336
TILE = 128
TOK_G = 128
KB = 16
FB = 112
FBL = 7
GT = 112
CAP = 13
TOKENS = 2048
N_DP = 16
N_TENSOR = 16


def draw_tile_owner(key, part):
    group_tiles = FBL * KB
    spare_owners = N_DP - 1
    owner_quota = -(-(group_tiles - CAP) // spare_owners)
    group_keys = jax.random.split(key, 2 * N_TENSOR)

    def one_group(group_key):
        first_key, second_key, third_key = jax.random.split(group_key, 3)
        busiest = jax.random.randint(first_key, (), 0, N_DP).astype(jnp.int32)
        placing = jax.random.permutation(second_key, group_tiles).astype(jnp.int32)
        spread = (jax.random.permutation(third_key, spare_owners * owner_quota).astype(jnp.int32)[:group_tiles - CAP] // owner_quota).astype(jnp.int32)
        others = spread + (spread >= busiest).astype(jnp.int32)
        sequence = jnp.concatenate([jnp.full((CAP,), 1, jnp.int32) * busiest, others.astype(jnp.int32)])
        return sequence[placing]
    owners = jax.vmap(one_group)(group_keys)
    return owners.reshape(2, N_TENSOR * FBL, KB).astype(jnp.int32)


def level_of(own_key, extent, pieces, smallest, top_value):
    gain, own = 1.0, jax.random.fold_in(own_key, 6)
    for position, parts in pieces:
        draws = jnp.exp(jax.random.uniform(jax.random.fold_in(own, position), (parts,), jnp.float32, smallest / len(pieces), top_value / len(pieces)))
        gain = gain * jnp.repeat(draws, extent[position] // parts).reshape([-1 if axis == position else 1 for axis in range(len(extent))])
    return gain


def choose_distinct(rng, rows, amount, top, lift):
    ranking = jax.random.permutation(jax.random.fold_in(rng, 1), amount)
    favour = ranking
    for power in range(3):
        favour = favour * favour // amount
    favour = favour * lift // amount
    tickets = jax.random.randint(jax.random.fold_in(rng, 2), (rows, amount), 0, 4096) + favour
    fixed_rows = jax.random.permutation(jax.random.fold_in(rng, 3), rows)[jnp.arange(amount) % rows]
    tickets = jnp.where(jnp.arange(rows)[:, None] == fixed_rows[None, :], 1 << 14, tickets)
    merit = tickets * amount + jnp.arange(amount)
    return lax.top_k(merit.astype(jnp.int32), top)[1].astype(jnp.int32)


def noise(key, extent, scale, reach, shards=(), kind=jnp.bfloat16):
    array = jax.random.normal(key, extent, jnp.float32) * scale
    if len(shards) > 0:
        array = level_of(key, extent, shards, -0.22, 0.18) * array
    return jnp.clip(array, min=-reach, max=reach).astype(kind)


def setup_inputs(seed: int = 0) -> dict:
    key_of = jax.random.split(jax.random.key(seed), 7)
    tokens = noise(key_of[0], (TOKENS, D), 1.0, 6.0, ((0, 256),))
    hidden_grad = noise(key_of[1], (TOKENS, FF), 0.25, 1.5, ((0, 16), (1, 16)))
    gate_tiles = noise(key_of[2], (N_TENSOR, N_DP * CAP, TILE, TILE), (KB * TILE) ** -0.5, 0.125, ((0, 16), (1, 16)))
    up_tiles = noise(key_of[3], (N_TENSOR, N_DP * CAP, TILE, TILE), (KB * TILE) ** -0.5, 0.125, ((0, 16), (1, 16)))
    tile_rows = choose_distinct(key_of[4], 2 * FB, D // TILE, KB, 0).reshape((2, FB, KB))
    tile_owner = draw_tile_owner(jax.random.fold_in(key_of[6], 71), 0)
    return {"tokens": tokens, "hidden_grad": hidden_grad, "gate_tiles": gate_tiles, "up_tiles": up_tiles, "tile_rows": tile_rows, "tile_owner": tile_owner}


def slot_index(owner_ids):
    tile_total = owner_ids.shape[0]
    tile_order = jnp.arange(tile_total, dtype=jnp.int32)
    same_owner = (owner_ids[:, None] == owner_ids[None, :]) & (tile_order[None, :] < tile_order[:, None])
    tile_ranks = jnp.sum(same_owner.astype(jnp.int32), axis=1).astype(jnp.int32)
    return (owner_ids * CAP + tile_ranks).astype(jnp.int32)


def group_pass(tok_blocks, delta_hidden, gate_set, up_set, row_ids, owner_ids):
    row_count = D // TILE
    block_ids = (jnp.arange(GT, dtype=jnp.int32) // KB).astype(jnp.int32)
    tile_sets = (gate_set, up_set)
    slot_lists = []
    tile_panels = []
    picked_rows = []
    pre_acts = []
    for matrix_id in range(2):
        slot_list = slot_index(owner_ids[matrix_id].reshape(-1))
        tile_panel = jnp.take(tile_sets[matrix_id], slot_list, axis=0).astype(jnp.float32)
        picked = jnp.take(tok_blocks, row_ids[matrix_id].reshape(-1), axis=1).astype(jnp.float32)
        product = jnp.einsum('nir,irc->nic', picked, tile_panel)
        pre_acts.append(product.reshape(TOKENS, FBL, KB, TILE).sum(axis=2).reshape(TOKENS, FBL * TILE))
        slot_lists.append(slot_list)
        tile_panels.append(tile_panel)
        picked_rows.append(picked)
    gate_pre, up_pre = pre_acts
    hidden_part = (jax.nn.silu(gate_pre) * up_pre).astype(jnp.bfloat16)
    gate_sig = jax.nn.sigmoid(gate_pre)
    delta_full = delta_hidden.astype(jnp.float32)
    gate_delta = (delta_full * up_pre * gate_sig * (1.0 + gate_pre * (1.0 - gate_sig))).astype(jnp.bfloat16)
    up_delta = (delta_full * gate_pre * gate_sig).astype(jnp.bfloat16)
    deltas = (gate_delta, up_delta)
    token_sum = jnp.zeros((TOKENS, row_count, TILE), jnp.float32)
    grad_list = []
    for matrix_id in range(2):
        delta_blocks = deltas[matrix_id].reshape(TOKENS, FBL, TILE)
        delta_tiles = jnp.take(delta_blocks, block_ids, axis=1).astype(jnp.float32)
        back_rows = jnp.einsum('nic,irc->nir', delta_tiles, tile_panels[matrix_id])
        row_hot = (row_ids[matrix_id].reshape(-1)[:, None] == jnp.arange(row_count, dtype=jnp.int32)[None, :]).astype(jnp.float32)
        token_sum = token_sum + jnp.einsum('nir,ib->nbr', back_rows, row_hot, precision=lax.Precision.HIGHEST)
        picked_groups = picked_rows[matrix_id].reshape(N_DP, TOK_G, GT, TILE)
        delta_groups = delta_tiles.reshape(N_DP, TOK_G, GT, TILE)
        group_terms = jnp.einsum('gnir,gnic->girc', picked_groups, delta_groups).astype(jnp.bfloat16)
        group_terms = lax.optimization_barrier(group_terms).astype(jnp.float32)
        summed = jnp.sum(group_terms, axis=0)
        slot_buffer = jnp.zeros((N_DP * CAP, TILE, TILE), jnp.float32).at[slot_lists[matrix_id]].set(summed)
        grad_list.append(slot_buffer.astype(jnp.bfloat16))
    token_part = token_sum.reshape(TOKENS, D).astype(jnp.bfloat16)
    return hidden_part, token_part, jnp.stack(grad_list, axis=0)


def reference(tokens, hidden_grad, gate_tiles, up_tiles, tile_rows, tile_owner):
    tok_blocks = tokens.reshape(TOKENS, D // TILE, TILE)
    rows_grouped = tile_rows.reshape(2, N_TENSOR, FBL, KB).transpose(1, 0, 2, 3)
    owners_grouped = tile_owner.reshape(2, N_TENSOR, FBL, KB).transpose(1, 0, 2, 3)
    delta_grouped = hidden_grad.reshape(TOKENS, N_TENSOR, FBL * TILE).transpose(1, 0, 2)

    def group_step(token_total, group_args):
        gate_set, up_set, row_ids, owner_ids, delta_hidden = group_args
        hidden_part, token_part, grads = group_pass(tok_blocks, delta_hidden, gate_set, up_set, row_ids, owner_ids)
        token_part = lax.optimization_barrier(token_part)
        return token_total + token_part.astype(jnp.float32), (hidden_part, grads)

    start_total = jnp.zeros((TOKENS, D), jnp.float32)
    token_total, stacked = lax.scan(group_step, start_total, (gate_tiles, up_tiles, rows_grouped, owners_grouped, delta_grouped))
    hidden_parts, grad_parts = stacked
    hidden = hidden_parts.transpose(1, 0, 2).reshape(TOKENS, FF)
    return hidden, token_total.astype(jnp.bfloat16), grad_parts[:, 0], grad_parts[:, 1]
```

```python
import jax
import jax.numpy as jnp
from jax import lax
from jax.sharding import PartitionSpec as P


def slot_index(owner_ids, capacity):
    tile_total = owner_ids.shape[0]
    tile_order = jnp.arange(tile_total, dtype=jnp.int32)
    same_owner = (owner_ids[:, None] == owner_ids[None, :]) & (
        tile_order[None, :] < tile_order[:, None]
    )
    tile_ranks = jnp.sum(same_owner.astype(jnp.int32), axis=1)
    return owner_ids * capacity + tile_ranks


def body(tokens, hidden_grad, gate_tiles, up_tiles, tile_rows, tile_owner):
    tile_size = gate_tiles.shape[2]
    capacity = gate_tiles.shape[1]
    owner_count = lax.axis_size("dp")
    slot_total = capacity * owner_count
    tensor_count = lax.axis_size("tensor")
    tok_copies = jnp.broadcast_to(tokens[None], (tensor_count,) + tokens.shape)
    gathered_tok = lax.all_to_all(tok_copies, "tensor", 0, 0, tiled=True).reshape(
        tensor_count * tokens.shape[0], tokens.shape[1]
    )
    tok_count, model_width = gathered_tok.shape
    row_blocks = model_width // tile_size
    tok_blocks = gathered_tok.reshape(tok_count, row_blocks, tile_size)
    group_blocks = tile_rows.shape[1]
    per_block = tile_rows.shape[2]
    tile_count = group_blocks * per_block
    block_ids = jnp.arange(tile_count, dtype=jnp.int32) // per_block
    row_flat = tile_rows.reshape(2, tile_count)
    slot_stack = jnp.stack(
        [
            slot_index(tile_owner[0].reshape(-1), capacity),
            slot_index(tile_owner[1].reshape(-1), capacity),
        ],
        axis=0,
    )
    slot_grid = jnp.arange(slot_total, dtype=jnp.int32)
    slot_match = (slot_stack[:, None, :] == slot_grid[None, :, None]).astype(jnp.int32)
    slot_live = jnp.sum(slot_match, axis=2)
    slot_row = jnp.sum(slot_match * row_flat[:, None, :], axis=2)
    slot_block = jnp.sum(slot_match * block_ids[None, None, :], axis=2)
    slot_target = jnp.where(slot_live == 1, slot_block, group_blocks)
    local_gate = gate_tiles[0]
    local_up = up_tiles[0]
    gate_store, up_store = (
        lax.all_gather(local_gate, "dp", axis=0, tiled=True),
        lax.all_gather(local_up, "dp", axis=0, tiled=True),
    )
    gate_panel = jnp.take(gate_store, slot_stack[0], axis=0).reshape(
        group_blocks, per_block, tile_size, tile_size
    )
    up_panel = jnp.take(up_store, slot_stack[1], axis=0).reshape(
        group_blocks, per_block, tile_size, tile_size
    )
    picked = jnp.take(tok_blocks, row_flat.reshape(-1), axis=1).reshape(
        tok_count, 2, group_blocks, per_block, tile_size
    )
    gate_pre = jnp.einsum(
        "nfkr,fkrc->nfc", picked[:, 0], gate_panel, preferred_element_type=jnp.float32
    ).reshape(tok_count, group_blocks * tile_size)
    up_pre = jnp.einsum(
        "nfkr,fkrc->nfc", picked[:, 1], up_panel, preferred_element_type=jnp.float32
    ).reshape(tok_count, group_blocks * tile_size)
    hidden = (jax.nn.silu(gate_pre) * up_pre).astype(jnp.bfloat16)
    gate_sig = jax.nn.sigmoid(gate_pre)
    delta_full = hidden_grad.astype(jnp.float32)
    gate_delta = (delta_full * up_pre * gate_sig * (1.0 + gate_pre * (1.0 - gate_sig))).astype(
        jnp.bfloat16
    )
    up_delta = (delta_full * gate_pre * gate_sig).astype(jnp.bfloat16)
    delta_stack = jnp.stack(
        [
            gate_delta.reshape(tok_count, group_blocks, tile_size),
            up_delta.reshape(tok_count, group_blocks, tile_size),
        ],
        axis=1,
    )
    panel_stack = jnp.stack([gate_panel, up_panel], axis=0)
    back_rows = jnp.einsum(
        "nmfc,mfkrc->mfknr", delta_stack, panel_stack, preferred_element_type=jnp.float32
    )
    back_flat = back_rows.reshape(2 * tile_count, tok_count, tile_size)
    row_sums = jax.ops.segment_sum(back_flat, row_flat.reshape(-1), num_segments=row_blocks)
    token_part = row_sums.transpose(1, 0, 2).reshape(tok_count, model_width)
    part_rows = token_part.astype(jnp.bfloat16).reshape(tensor_count, tok_count // tensor_count, model_width)
    part_recv = lax.all_to_all(part_rows, "tensor", 0, 0, tiled=True)
    token_grad = jnp.sum(part_recv.astype(jnp.float32), axis=0).astype(jnp.bfloat16)
    zero_block = jnp.zeros((tok_count, 2, 1, tile_size), jnp.bfloat16)
    delta_padded = jnp.concatenate([delta_stack, zero_block], axis=2).reshape(
        tok_count, 2 * (group_blocks + 1), tile_size
    )
    matrix_base = jnp.arange(2, dtype=jnp.int32) * (group_blocks + 1)
    target_part = slot_target + matrix_base[:, None]
    chosen = jnp.take(tok_blocks, slot_row.reshape(-1), axis=1).reshape(
        tok_count, 2, capacity * lax.axis_size("dp"), tile_size
    )
    delta_part = jnp.take(delta_padded, target_part.reshape(-1), axis=1).reshape(
        tok_count, 2, capacity * lax.axis_size("dp"), tile_size
    )
    tile_sums = lax.psum_scatter(
        jnp.einsum(
            "nmsr,nmsc->smrc", chosen, delta_part, preferred_element_type=jnp.float32
        ).astype(jnp.bfloat16),
        "dp",
        scatter_dimension=0,
        tiled=True,
    ).astype(jnp.float32)
    gate_grad = tile_sums[:, 0].astype(jnp.bfloat16)[None]
    up_grad = tile_sums[:, 1].astype(jnp.bfloat16)[None]
    return (hidden, token_grad, gate_grad, up_grad)


def solution(mesh):
    placed = (
        P(("dp", "tensor"), None),
        P("dp", "tensor"),
        P("tensor", "dp", None, None),
        P("tensor", "dp", None, None),
        P(None, "tensor", None),
        P(None, "tensor", None),
    )
    return jax.shard_map(
        body,
        mesh=mesh,
        in_specs=placed,
        out_specs=(
            P("dp", "tensor"),
            P(("dp", "tensor"), None),
            P("tensor", "dp", None, None),
            P("tensor", "dp", None, None),
        ),
        check_vma=False,
    )
```

```python
import jax
import jax.numpy as jnp
from jax import lax
from jax.experimental import pallas as pl
from jax.experimental.pallas import tpu as pltpu
from jax.sharding import PartitionSpec as P


def slot_index(owner_ids, capacity):
    tile_total = owner_ids.shape[0]
    tile_order = jnp.arange(tile_total, dtype=jnp.int32)
    same_owner = (owner_ids[:, None] == owner_ids[None, :]) & (
        tile_order[None, :] < tile_order[:, None]
    )
    tile_ranks = jnp.sum(same_owner.astype(jnp.int32), axis=1)
    return owner_ids * capacity + tile_ranks


def _swiglu_kernel(rows_ref, slots_ref, tok_ref, tokt_ref, gstore_ref, ustore_ref, hgrad_ref,
                   hidden_ref, tpart_ref, grad_ref, acc_ref, delta_ref):
    group_blocks = hgrad_ref.shape[1] // 128
    per_block = rows_ref.shape[1] // group_blocks
    stores = (gstore_ref, ustore_ref)
    acc_ref[...] = jnp.zeros(acc_ref.shape, jnp.float32)
    grad_ref[...] = jnp.zeros(grad_ref.shape, grad_ref.dtype)
    for f in range(group_blocks):
        pre = []
        for m in range(2):
            def fwd_step(k, carry, m=m):
                i = f * per_block + k
                r = rows_ref[m, i]
                s = slots_ref[m, i]
                return carry + jnp.dot(tok_ref[r], stores[m][s], preferred_element_type=jnp.float32)
            pre.append(lax.fori_loop(0, per_block, fwd_step,
                                     jnp.zeros((128, 128), jnp.float32), unroll=True))
        gate_pre, up_pre = pre
        cols = slice(f * 128, (f + 1) * 128)
        hg = hgrad_ref[:, cols].astype(jnp.float32)
        sig = 1.0 / (1.0 + jnp.exp(-gate_pre))
        hidden_ref[:, cols] = (gate_pre * sig * up_pre).astype(hidden_ref.dtype)
        delta_ref[0] = (hg * up_pre * sig * (1.0 + gate_pre * (1.0 - sig))).astype(delta_ref.dtype)
        delta_ref[1] = (hg * gate_pre * sig).astype(delta_ref.dtype)

        def back_step(k, carry):
            i = f * per_block + k
            for m in range(2):
                r = rows_ref[m, i]
                s = slots_ref[m, i]
                d = delta_ref[m]
                back = lax.dot_general(d, stores[m][s], (((1,), (1,)), ((), ())),
                                       preferred_element_type=jnp.float32)
                acc_ref[r] = acc_ref[r] + back
                term = jnp.dot(tokt_ref[r], d, preferred_element_type=jnp.float32)
                grad_ref[s, m] = term.astype(grad_ref.dtype)
            return carry
        lax.fori_loop(0, per_block, back_step, 0, unroll=True)
    tpart_ref[...] = acc_ref[...].astype(tpart_ref.dtype)


def swiglu_local(rows, slots, tok_bm, tokt_bm, gstore, ustore, hgrad, interpret=False):
    row_blocks, tok_count, tile = tok_bm.shape
    slot_total = gstore.shape[0]
    smem = pl.BlockSpec(memory_space=pltpu.SMEM)
    vmem = pl.BlockSpec(memory_space=pltpu.VMEM)
    out_shape = (
        jax.ShapeDtypeStruct(hgrad.shape, jnp.bfloat16),
        jax.ShapeDtypeStruct((row_blocks, tok_count, tile), jnp.bfloat16),
        jax.ShapeDtypeStruct((slot_total, 2, tile, tile), jnp.bfloat16),
    )
    return pl.pallas_call(
        _swiglu_kernel,
        out_shape=out_shape,
        in_specs=[smem, smem, vmem, vmem, vmem, vmem, vmem],
        out_specs=(vmem, vmem, vmem),
        scratch_shapes=[pltpu.VMEM((row_blocks, tok_count, tile), jnp.float32),
                        pltpu.VMEM((2, tok_count, tile), jnp.bfloat16)],
        compiler_params=pltpu.CompilerParams(vmem_limit_bytes=100 * 1024 * 1024),
        interpret=interpret,
    )(rows, slots, tok_bm, tokt_bm, gstore, ustore, hgrad)


def body(tokens, hidden_grad, gate_tiles, up_tiles, tile_rows, tile_owner):
    tile_size = gate_tiles.shape[2]
    capacity = gate_tiles.shape[1]
    tensor_count = lax.axis_size("tensor")
    tok_copies = jnp.broadcast_to(tokens[None], (tensor_count,) + tokens.shape)
    gathered_tok = lax.all_to_all(tok_copies, "tensor", 0, 0, tiled=True).reshape(
        tensor_count * tokens.shape[0], tokens.shape[1]
    )
    tok_count, model_width = gathered_tok.shape
    row_blocks = model_width // tile_size
    tok_blocks = gathered_tok.reshape(tok_count, row_blocks, tile_size)
    tok_bm = tok_blocks.transpose(1, 0, 2)
    tokt_bm = tok_blocks.transpose(1, 2, 0)
    tile_count = tile_rows.shape[1] * tile_rows.shape[2]
    row_flat = tile_rows.reshape(2, tile_count)
    slot_stack = jnp.stack(
        [
            slot_index(tile_owner[0].reshape(-1), capacity),
            slot_index(tile_owner[1].reshape(-1), capacity),
        ],
        axis=0,
    )
    gate_store = lax.all_gather(gate_tiles[0], "dp", axis=0, tiled=True)
    up_store = lax.all_gather(up_tiles[0], "dp", axis=0, tiled=True)
    hidden, tpart_bm, grads = swiglu_local(
        row_flat, slot_stack, tok_bm, tokt_bm, gate_store, up_store, hidden_grad
    )
    token_part = tpart_bm.transpose(1, 0, 2).reshape(tok_count, model_width)
    part_rows = token_part.reshape(tensor_count, tok_count // tensor_count, model_width)
    part_recv = lax.all_to_all(part_rows, "tensor", 0, 0, tiled=True)
    token_grad = jnp.sum(part_recv.astype(jnp.float32), axis=0).astype(jnp.bfloat16)
    tile_sums = lax.psum_scatter(grads, "dp", scatter_dimension=0, tiled=True)
    gate_grad = tile_sums[:, 0][None]
    up_grad = tile_sums[:, 1][None]
    return (hidden, token_grad, gate_grad, up_grad)


def solution(mesh):
    placed = (
        P(("dp", "tensor"), None),
        P("dp", "tensor"),
        P("tensor", "dp", None, None),
        P("tensor", "dp", None, None),
        P(None, "tensor", None),
        P(None, "tensor", None),
    )
    return jax.shard_map(
        body,
        mesh=mesh,
        in_specs=placed,
        out_specs=(
            P("dp", "tensor"),
            P(("dp", "tensor"), None),
            P("tensor", "dp", None, None),
            P("tensor", "dp", None, None),
        ),
        check_vma=False,
    )
```

```python
import jax
import jax.numpy as jnp
from jax import lax
from jax.experimental import pallas as pl
from jax.experimental.pallas import tpu as pltpu
from jax.sharding import PartitionSpec as P


def slot_index(owner_ids, capacity, core_count, chip_count):
    tile_total = owner_ids.shape[0]
    tile_order = jnp.arange(tile_total, dtype=jnp.int32)
    same_owner = (owner_ids[:, None] == owner_ids[None, :]) & (
        tile_order[None, :] < tile_order[:, None]
    )
    tile_ranks = jnp.sum(same_owner.astype(jnp.int32), axis=1)
    owner_core = owner_ids % core_count
    owner_chip = owner_ids // core_count
    return (owner_core * chip_count + owner_chip) * capacity + tile_ranks


def _swiglu_kernel(rows_ref, slots_ref, tok_ref, tokt_ref, gstore_ref, ustore_ref, hgrad_ref,
                   hidden_ref, tpart_ref, grad_ref, acc_ref, delta_ref):
    group_blocks = hgrad_ref.shape[1] // 128
    per_block = rows_ref.shape[1] // group_blocks
    stores = (gstore_ref, ustore_ref)
    acc_ref[...] = jnp.zeros(acc_ref.shape, jnp.float32)
    grad_ref[...] = jnp.zeros(grad_ref.shape, grad_ref.dtype)
    for f in range(group_blocks):
        pre = []
        for m in range(2):
            def fwd_step(k, carry, m=m):
                i = f * per_block + k
                r = rows_ref[m, i]
                s = slots_ref[m, i]
                return carry + jnp.dot(tok_ref[r], stores[m][s], preferred_element_type=jnp.float32)
            pre.append(lax.fori_loop(0, per_block, fwd_step,
                                     jnp.zeros((128, 128), jnp.float32), unroll=True))
        gate_pre, up_pre = pre
        cols = slice(f * 128, (f + 1) * 128)
        hg = hgrad_ref[:, cols].astype(jnp.float32)
        sig = 1.0 / (1.0 + jnp.exp(-gate_pre))
        hidden_ref[:, cols] = (gate_pre * sig * up_pre).astype(hidden_ref.dtype)
        delta_ref[0] = (hg * up_pre * sig * (1.0 + gate_pre * (1.0 - sig))).astype(delta_ref.dtype)
        delta_ref[1] = (hg * gate_pre * sig).astype(delta_ref.dtype)

        def back_step(k, carry):
            i = f * per_block + k
            for m in range(2):
                r = rows_ref[m, i]
                s = slots_ref[m, i]
                d = delta_ref[m]
                back = lax.dot_general(d, stores[m][s], (((1,), (1,)), ((), ())),
                                       preferred_element_type=jnp.float32)
                acc_ref[r] = acc_ref[r] + back
                term = jnp.dot(tokt_ref[r], d, preferred_element_type=jnp.float32)
                grad_ref[s, m] = term.astype(grad_ref.dtype)
            return carry
        lax.fori_loop(0, per_block, back_step, 0, unroll=True)
    tpart_ref[...] = acc_ref[...].astype(tpart_ref.dtype)


def swiglu_local(rows, slots, tok_bm, tokt_bm, gstore, ustore, hgrad, interpret=False):
    row_blocks, tok_count, tile = tok_bm.shape
    slot_total = gstore.shape[0]
    smem = pl.BlockSpec(memory_space=pltpu.SMEM)
    vmem = pl.BlockSpec(memory_space=pltpu.VMEM)
    out_shape = (
        jax.ShapeDtypeStruct(hgrad.shape, jnp.bfloat16),
        jax.ShapeDtypeStruct((row_blocks, tok_count, tile), jnp.bfloat16),
        jax.ShapeDtypeStruct((slot_total, 2, tile, tile), jnp.bfloat16),
    )
    return pl.pallas_call(
        _swiglu_kernel,
        out_shape=out_shape,
        in_specs=[smem, smem, vmem, vmem, vmem, vmem, vmem],
        out_specs=(vmem, vmem, vmem),
        scratch_shapes=[pltpu.VMEM((row_blocks, tok_count, tile), jnp.float32),
                        pltpu.VMEM((2, tok_count, tile), jnp.bfloat16)],
        compiler_params=pltpu.CompilerParams(vmem_limit_bytes=100 * 1024 * 1024),
        interpret=interpret,
    )(rows, slots, tok_bm, tokt_bm, gstore, ustore, hgrad)


def body(tokens, hidden_grad, gate_tiles, up_tiles, tile_rows, tile_owner):
    tile_size = gate_tiles.shape[2]
    capacity = gate_tiles.shape[1]
    tensor_count = lax.axis_size("tensor")
    tok_copies = jnp.broadcast_to(tokens[None], (tensor_count,) + tokens.shape)
    gathered_tok = lax.all_to_all(tok_copies, "tensor", 0, 0, tiled=True).reshape(
        tensor_count * tokens.shape[0], tokens.shape[1]
    )
    tok_count, model_width = gathered_tok.shape
    row_blocks = model_width // tile_size
    tok_blocks = gathered_tok.reshape(tok_count, row_blocks, tile_size)
    tok_bm = tok_blocks.transpose(1, 0, 2)
    tokt_bm = tok_blocks.transpose(1, 2, 0)
    tile_count = tile_rows.shape[1] * tile_rows.shape[2]
    row_flat = tile_rows.reshape(2, tile_count)
    core_count = lax.axis_size("core")
    chip_count = lax.axis_size("z")
    slot_stack = jnp.stack(
        [
            slot_index(tile_owner[0].reshape(-1), capacity, core_count, chip_count),
            slot_index(tile_owner[1].reshape(-1), capacity, core_count, chip_count),
        ],
        axis=0,
    )
    gate_store = lax.all_gather(
        lax.all_gather(gate_tiles[0], "z", axis=0, tiled=True), "core", axis=0, tiled=True
    )
    up_store = lax.all_gather(
        lax.all_gather(up_tiles[0], "z", axis=0, tiled=True), "core", axis=0, tiled=True
    )
    hidden, tpart_bm, grads = swiglu_local(
        row_flat, slot_stack, tok_bm, tokt_bm, gate_store, up_store, hidden_grad
    )
    token_part = tpart_bm.transpose(1, 0, 2).reshape(tok_count, model_width)
    part_rows = token_part.reshape(tensor_count, tok_count // tensor_count, model_width)
    part_recv = lax.all_to_all(part_rows, "tensor", 0, 0, tiled=True)
    token_grad = jnp.sum(part_recv.astype(jnp.float32), axis=0).astype(jnp.bfloat16)
    core_sums = lax.psum_scatter(grads, "core", scatter_dimension=0, tiled=True)
    tile_sums = lax.psum_scatter(core_sums, "z", scatter_dimension=0, tiled=True)
    gate_grad = tile_sums[:, 0][None]
    up_grad = tile_sums[:, 1][None]
    return (hidden, token_grad, gate_grad, up_grad)


def solution(mesh):
    dp_size = mesh.shape["dp"]
    chip_count = dp_size // 2
    split_mesh = jax.sharding.Mesh(
        mesh.devices.reshape(chip_count, 2, mesh.shape["tensor"]), ("z", "core", "tensor")
    )
    dp = ("z", "core")
    placed = (
        P(dp + ("tensor",), None),
        P(dp, "tensor"),
        P("tensor", dp, None, None),
        P("tensor", dp, None, None),
        P(None, "tensor", None),
        P(None, "tensor", None),
    )
    return jax.shard_map(
        body,
        mesh=split_mesh,
        in_specs=placed,
        out_specs=(
            P(dp, "tensor"),
            P(dp + ("tensor",), None),
            P("tensor", dp, None, None),
            P("tensor", dp, None, None),
        ),
        check_vma=False,
    )
```

```python
import jax
import jax.numpy as jnp
from jax import lax
from jax.experimental import pallas as pl
from jax.experimental.pallas import tpu as pltpu
from jax.sharding import PartitionSpec as P


def slot_index(owner_ids, capacity):
    tile_total = owner_ids.shape[0]
    tile_order = jnp.arange(tile_total, dtype=jnp.int32)
    same_owner = (owner_ids[:, None] == owner_ids[None, :]) & (
        tile_order[None, :] < tile_order[:, None]
    )
    tile_ranks = jnp.sum(same_owner.astype(jnp.int32), axis=1)
    return owner_ids * capacity + tile_ranks


def _swiglu_kernel(rows_ref, slots_ref, tok_ref, tokt_ref, store_ref, hgrad_ref,
                   hidden_ref, tpart_ref, grad_ref, acc_ref, delta_ref):
    group_blocks = hgrad_ref.shape[1] // 128
    per_block = rows_ref.shape[1] // group_blocks
    acc_ref[...] = jnp.zeros(acc_ref.shape, jnp.float32)
    grad_ref[...] = jnp.zeros(grad_ref.shape, grad_ref.dtype)
    for f in range(group_blocks):
        pre = []
        for m in range(2):
            def fwd_step(k, carry, m=m):
                i = f * per_block + k
                r = rows_ref[m, i]
                s = slots_ref[m, i]
                return carry + jnp.dot(tok_ref[r], store_ref[s, m], preferred_element_type=jnp.float32)
            pre.append(lax.fori_loop(0, per_block, fwd_step,
                                     jnp.zeros((128, 128), jnp.float32), unroll=True))
        gate_pre, up_pre = pre
        cols = slice(f * 128, (f + 1) * 128)
        hg = hgrad_ref[:, cols].astype(jnp.float32)
        sig = 1.0 / (1.0 + jnp.exp(-gate_pre))
        hidden_ref[:, cols] = (gate_pre * sig * up_pre).astype(hidden_ref.dtype)
        delta_ref[0] = (hg * up_pre * sig * (1.0 + gate_pre * (1.0 - sig))).astype(delta_ref.dtype)
        delta_ref[1] = (hg * gate_pre * sig).astype(delta_ref.dtype)

        def back_step(k, carry):
            i = f * per_block + k
            for m in range(2):
                r = rows_ref[m, i]
                s = slots_ref[m, i]
                d = delta_ref[m]
                back = lax.dot_general(d, store_ref[s, m], (((1,), (1,)), ((), ())),
                                       preferred_element_type=jnp.float32)
                acc_ref[r] = acc_ref[r] + back
                term = jnp.dot(tokt_ref[r], d, preferred_element_type=jnp.float32)
                grad_ref[s, m] = term.astype(grad_ref.dtype)
            return carry
        lax.fori_loop(0, per_block, back_step, 0, unroll=True)
    tpart_ref[...] = acc_ref[...].astype(tpart_ref.dtype)


def swiglu_local(rows, slots, tok_bm, tokt_bm, store, hgrad, interpret=False):
    row_blocks, tok_count, tile = tok_bm.shape
    slot_total = store.shape[0]
    smem = pl.BlockSpec(memory_space=pltpu.SMEM)
    vmem = pl.BlockSpec(memory_space=pltpu.VMEM)
    out_shape = (
        jax.ShapeDtypeStruct(hgrad.shape, jnp.bfloat16),
        jax.ShapeDtypeStruct((row_blocks, tok_count, tile), jnp.bfloat16),
        jax.ShapeDtypeStruct((slot_total, 2, tile, tile), jnp.bfloat16),
    )
    return pl.pallas_call(
        _swiglu_kernel,
        out_shape=out_shape,
        in_specs=[smem, smem, vmem, vmem, vmem, vmem],
        out_specs=(vmem, vmem, vmem),
        scratch_shapes=[pltpu.VMEM((row_blocks, tok_count, tile), jnp.float32),
                        pltpu.VMEM((2, tok_count, tile), jnp.bfloat16)],
        compiler_params=pltpu.CompilerParams(vmem_limit_bytes=100 * 1024 * 1024),
        interpret=interpret,
    )(rows, slots, tok_bm, tokt_bm, store, hgrad)


def body(tokens, hidden_grad, gate_tiles, up_tiles, tile_rows, tile_owner):
    tile_size = gate_tiles.shape[2]
    capacity = gate_tiles.shape[1]
    tensor_count = lax.axis_size("tensor")
    tok_copies = jnp.broadcast_to(tokens[None], (tensor_count,) + tokens.shape)
    gathered_tok = lax.all_to_all(tok_copies, "tensor", 0, 0, tiled=True).reshape(
        tensor_count * tokens.shape[0], tokens.shape[1]
    )
    tok_count, model_width = gathered_tok.shape
    row_blocks = model_width // tile_size
    tok_blocks = gathered_tok.reshape(tok_count, row_blocks, tile_size)
    tok_bm = tok_blocks.transpose(1, 0, 2)
    tokt_bm = tok_blocks.transpose(1, 2, 0)
    tile_count = tile_rows.shape[1] * tile_rows.shape[2]
    row_flat = tile_rows.reshape(2, tile_count)
    slot_stack = jnp.stack(
        [
            slot_index(tile_owner[0].reshape(-1), capacity),
            slot_index(tile_owner[1].reshape(-1), capacity),
        ],
        axis=0,
    )
    local_pair = jnp.stack([gate_tiles[0], up_tiles[0]], axis=1)
    store = lax.all_gather(local_pair, "dp", axis=0, tiled=True)
    hidden, tpart_bm, grads = swiglu_local(
        row_flat, slot_stack, tok_bm, tokt_bm, store, hidden_grad
    )
    token_part = tpart_bm.transpose(1, 0, 2).reshape(tok_count, model_width)
    part_rows = token_part.reshape(tensor_count, tok_count // tensor_count, model_width)
    part_recv = lax.all_to_all(part_rows, "tensor", 0, 0, tiled=True)
    token_grad = jnp.sum(part_recv.astype(jnp.float32), axis=0).astype(jnp.bfloat16)
    tile_sums = lax.psum_scatter(grads, "dp", scatter_dimension=0, tiled=True)
    gate_grad = tile_sums[:, 0][None]
    up_grad = tile_sums[:, 1][None]
    return (hidden, token_grad, gate_grad, up_grad)


def solution(mesh):
    placed = (
        P(("dp", "tensor"), None),
        P("dp", "tensor"),
        P("tensor", "dp", None, None),
        P("tensor", "dp", None, None),
        P(None, "tensor", None),
        P(None, "tensor", None),
    )
    return jax.shard_map(
        body,
        mesh=mesh,
        in_specs=placed,
        out_specs=(
            P("dp", "tensor"),
            P(("dp", "tensor"), None),
            P("tensor", "dp", None, None),
            P("tensor", "dp", None, None),
        ),
        check_vma=False,
    )
```

```python
import jax
import jax.numpy as jnp
from jax import lax
from jax.experimental import pallas as pl
from jax.experimental.pallas import tpu as pltpu
from jax.sharding import PartitionSpec as P


def slot_index(owner_ids, capacity):
    tile_total = owner_ids.shape[0]
    tile_order = jnp.arange(tile_total, dtype=jnp.int32)
    same_owner = (owner_ids[:, None] == owner_ids[None, :]) & (
        tile_order[None, :] < tile_order[:, None]
    )
    tile_ranks = jnp.sum(same_owner.astype(jnp.int32), axis=1)
    return owner_ids * capacity + tile_ranks


def _swiglu_kernel(rows_ref, slots_ref, tok_ref, tokt_ref, store_hbm, hgrad_ref, zero_hbm,
                   hidden_ref, tpart_ref, grad_hbm, acc_ref, delta_ref, panel_ref, term_ref,
                   in_sem, out_sem):
    del zero_hbm
    group_blocks = hgrad_ref.shape[1] // 128
    tile_count = rows_ref.shape[1]
    per_block = tile_count // group_blocks

    def tile_copy_in(m, i):
        s = slots_ref[m, i]
        return pltpu.make_async_copy(store_hbm.at[s, m], panel_ref.at[m, i],
                                     in_sem.at[m * tile_count + i])

    def tile_copy_out(m, i):
        s = slots_ref[m, i]
        return pltpu.make_async_copy(term_ref.at[m, i], grad_hbm.at[s, m],
                                     out_sem.at[m * tile_count + i])

    def start_in(i, carry):
        for m in range(2):
            tile_copy_in(m, i).start()
        return carry
    lax.fori_loop(0, tile_count, start_in, 0)
    acc_ref[...] = jnp.zeros(acc_ref.shape, jnp.float32)
    for f in range(group_blocks):
        def wait_in(k, carry, f=f):
            for m in range(2):
                tile_copy_in(m, f * per_block + k).wait()
            return carry
        lax.fori_loop(0, per_block, wait_in, 0)
        pre = []
        for m in range(2):
            def fwd_step(k, carry, m=m, f=f):
                i = f * per_block + k
                r = rows_ref[m, i]
                return carry + jnp.dot(tok_ref[r], panel_ref[m, i],
                                       preferred_element_type=jnp.float32)
            pre.append(lax.fori_loop(0, per_block, fwd_step,
                                     jnp.zeros((128, 128), jnp.float32), unroll=True))
        gate_pre, up_pre = pre
        cols = slice(f * 128, (f + 1) * 128)
        hg = hgrad_ref[:, cols].astype(jnp.float32)
        sig = 1.0 / (1.0 + jnp.exp(-gate_pre))
        hidden_ref[:, cols] = (gate_pre * sig * up_pre).astype(hidden_ref.dtype)
        delta_ref[0] = (hg * up_pre * sig * (1.0 + gate_pre * (1.0 - sig))).astype(delta_ref.dtype)
        delta_ref[1] = (hg * gate_pre * sig).astype(delta_ref.dtype)

        def back_step(k, carry, f=f):
            i = f * per_block + k
            for m in range(2):
                r = rows_ref[m, i]
                d = delta_ref[m]
                back = lax.dot_general(d, panel_ref[m, i], (((1,), (1,)), ((), ())),
                                       preferred_element_type=jnp.float32)
                acc_ref[r] = acc_ref[r] + back
                term = jnp.dot(tokt_ref[r], d, preferred_element_type=jnp.float32)
                term_ref[m, i] = term.astype(term_ref.dtype)
                tile_copy_out(m, i).start()
            return carry
        lax.fori_loop(0, per_block, back_step, 0, unroll=True)
    tpart_ref[...] = acc_ref[...].astype(tpart_ref.dtype)

    def wait_out(i, carry):
        for m in range(2):
            tile_copy_out(m, i).wait()
        return carry
    lax.fori_loop(0, tile_count, wait_out, 0)


def swiglu_local(rows, slots, tok_bm, tokt_bm, store, hgrad, interpret=False):
    row_blocks, tok_count, tile = tok_bm.shape
    tile_count = rows.shape[1]
    smem = pl.BlockSpec(memory_space=pltpu.SMEM)
    vmem = pl.BlockSpec(memory_space=pltpu.VMEM)
    hbm = pl.BlockSpec(memory_space=pl.ANY)
    zero_grads = jnp.zeros(store.shape, jnp.bfloat16)
    out_shape = (
        jax.ShapeDtypeStruct(hgrad.shape, jnp.bfloat16),
        jax.ShapeDtypeStruct((row_blocks, tok_count, tile), jnp.bfloat16),
        jax.ShapeDtypeStruct(store.shape, jnp.bfloat16),
    )
    return pl.pallas_call(
        _swiglu_kernel,
        out_shape=out_shape,
        in_specs=[smem, smem, vmem, vmem, hbm, vmem, hbm],
        out_specs=(vmem, vmem, hbm),
        scratch_shapes=[pltpu.VMEM((row_blocks, tok_count, tile), jnp.float32),
                        pltpu.VMEM((2, tok_count, tile), jnp.bfloat16),
                        pltpu.VMEM((2, tile_count, tile, tile), jnp.bfloat16),
                        pltpu.VMEM((2, tile_count, tile, tile), jnp.bfloat16),
                        pltpu.SemaphoreType.DMA((2 * tile_count,)),
                        pltpu.SemaphoreType.DMA((2 * tile_count,))],
        input_output_aliases={6: 2},
        compiler_params=pltpu.CompilerParams(vmem_limit_bytes=100 * 1024 * 1024),
        interpret=interpret,
    )(rows, slots, tok_bm, tokt_bm, store, hgrad, zero_grads)


def body(tokens, hidden_grad, gate_tiles, up_tiles, tile_rows, tile_owner):
    tile_size = gate_tiles.shape[2]
    capacity = gate_tiles.shape[1]
    tensor_count = lax.axis_size("tensor")
    tok_copies = jnp.broadcast_to(tokens[None], (tensor_count,) + tokens.shape)
    gathered_tok = lax.all_to_all(tok_copies, "tensor", 0, 0, tiled=True).reshape(
        tensor_count * tokens.shape[0], tokens.shape[1]
    )
    tok_count, model_width = gathered_tok.shape
    row_blocks = model_width // tile_size
    tok_blocks = gathered_tok.reshape(tok_count, row_blocks, tile_size)
    tok_bm = tok_blocks.transpose(1, 0, 2)
    tokt_bm = tok_blocks.transpose(1, 2, 0)
    tile_count = tile_rows.shape[1] * tile_rows.shape[2]
    row_flat = tile_rows.reshape(2, tile_count)
    slot_stack = jnp.stack(
        [
            slot_index(tile_owner[0].reshape(-1), capacity),
            slot_index(tile_owner[1].reshape(-1), capacity),
        ],
        axis=0,
    )
    local_pair = jnp.stack([gate_tiles[0], up_tiles[0]], axis=1)
    store = lax.all_gather(local_pair, "dp", axis=0, tiled=True)
    hidden, tpart_bm, grads = swiglu_local(
        row_flat, slot_stack, tok_bm, tokt_bm, store, hidden_grad
    )
    token_part = tpart_bm.transpose(1, 0, 2).reshape(tok_count, model_width)
    part_rows = token_part.reshape(tensor_count, tok_count // tensor_count, model_width)
    part_recv = lax.all_to_all(part_rows, "tensor", 0, 0, tiled=True)
    token_grad = jnp.sum(part_recv.astype(jnp.float32), axis=0).astype(jnp.bfloat16)
    tile_sums = lax.psum_scatter(grads, "dp", scatter_dimension=0, tiled=True)
    gate_grad = tile_sums[:, 0][None]
    up_grad = tile_sums[:, 1][None]
    return (hidden, token_grad, gate_grad, up_grad)


def solution(mesh):
    placed = (
        P(("dp", "tensor"), None),
        P("dp", "tensor"),
        P("tensor", "dp", None, None),
        P("tensor", "dp", None, None),
        P(None, "tensor", None),
        P(None, "tensor", None),
    )
    return jax.shard_map(
        body,
        mesh=mesh,
        in_specs=placed,
        out_specs=(
            P("dp", "tensor"),
            P(("dp", "tensor"), None),
            P("tensor", "dp", None, None),
            P("tensor", "dp", None, None),
        ),
        check_vma=False,
    )
```

```python
import jax
import jax.numpy as jnp
from jax import lax
from jax.experimental import pallas as pl
from jax.experimental.pallas import tpu as pltpu
from jax.sharding import PartitionSpec as P


def slot_index(owner_ids, capacity):
    tile_total = owner_ids.shape[0]
    tile_order = jnp.arange(tile_total, dtype=jnp.int32)
    same_owner = (owner_ids[:, None] == owner_ids[None, :]) & (
        tile_order[None, :] < tile_order[:, None]
    )
    tile_ranks = jnp.sum(same_owner.astype(jnp.int32), axis=1)
    return owner_ids * capacity + tile_ranks


def _swiglu_kernel(rows_ref, slots_ref, free_ref, tok_ref, tokt_ref, store_hbm, hgrad_ref,
                   hidden_ref, tpart_ref, grad_hbm, acc_ref, panel_ref, term_ref, picked_ref,
                   zero_ref, in_sem, out_sem, zero_sem):
    group_blocks = hgrad_ref.shape[1] // 128
    tile_count = rows_ref.shape[1]
    free_count = free_ref.shape[1]
    per_block = tile_count // group_blocks
    tile = panel_ref.shape[2]

    def tile_copy_in(m, i):
        s = slots_ref[m, i]
        return pltpu.make_async_copy(store_hbm.at[s, m], panel_ref.at[m, i],
                                     in_sem.at[m * tile_count + i])

    def tile_copy_out(m, i):
        s = slots_ref[m, i]
        return pltpu.make_async_copy(term_ref.at[m, i], grad_hbm.at[s, m],
                                     out_sem.at[m * tile_count + i])

    def zero_copy(m, j):
        u = free_ref[m, j]
        return pltpu.make_async_copy(zero_ref, grad_hbm.at[u, m], zero_sem.at[m * free_count + j])

    def start_in(i, carry):
        for m in range(2):
            tile_copy_in(m, i).start()
        return carry
    lax.fori_loop(0, tile_count, start_in, 0)
    zero_ref[...] = jnp.zeros(zero_ref.shape, zero_ref.dtype)

    def start_zero(j, carry):
        for m in range(2):
            zero_copy(m, j).start()
        return carry
    lax.fori_loop(0, free_count, start_zero, 0)
    acc_ref[...] = jnp.zeros(acc_ref.shape, jnp.float32)
    for f in range(group_blocks):
        def wait_in(k, carry, f=f):
            for m in range(2):
                tile_copy_in(m, f * per_block + k).wait()
            return carry
        lax.fori_loop(0, per_block, wait_in, 0)
        pre = []
        for m in range(2):
            def fwd_step(k, carry, m=m, f=f):
                i = f * per_block + k
                r = rows_ref[m, i]
                return carry + jnp.dot(tok_ref[r], panel_ref[m, i],
                                       preferred_element_type=jnp.float32)
            pre.append(lax.fori_loop(0, per_block, fwd_step,
                                     jnp.zeros((tile, tile), jnp.float32), unroll=True))
        gate_pre, up_pre = pre
        cols = slice(f * tile, (f + 1) * tile)
        hg = hgrad_ref[:, cols].astype(jnp.float32)
        sig = 1.0 / (1.0 + jnp.exp(-gate_pre))
        hidden_ref[:, cols] = (gate_pre * sig * up_pre).astype(hidden_ref.dtype)
        gate_delta = (hg * up_pre * sig * (1.0 + gate_pre * (1.0 - sig))).astype(jnp.bfloat16)
        up_delta = (hg * gate_pre * sig).astype(jnp.bfloat16)
        for m, delta in ((0, gate_delta), (1, up_delta)):
            delta_t = delta.astype(jnp.float32).T.astype(jnp.bfloat16)
            for k in range(per_block):
                r = rows_ref[m, f * per_block + k]
                picked_ref[k * tile:(k + 1) * tile, :] = tokt_ref[r]
            panel = panel_ref[m, f * per_block:(f + 1) * per_block].reshape(per_block * tile, tile)
            back_t = jnp.dot(panel, delta_t, preferred_element_type=jnp.float32)
            term = jnp.dot(picked_ref[...], delta, preferred_element_type=jnp.float32)
            for k in range(per_block):
                i = f * per_block + k
                r = rows_ref[m, i]
                acc_ref[r] = acc_ref[r] + back_t[k * tile:(k + 1) * tile]
                term_ref[m, i] = term[k * tile:(k + 1) * tile].astype(term_ref.dtype)
                tile_copy_out(m, i).start()
    tpart_ref[...] = acc_ref[...].astype(tpart_ref.dtype)

    def wait_out(i, carry):
        for m in range(2):
            tile_copy_out(m, i).wait()
        return carry
    lax.fori_loop(0, tile_count, wait_out, 0)

    def wait_zero(j, carry):
        for m in range(2):
            zero_copy(m, j).wait()
        return carry
    lax.fori_loop(0, free_count, wait_zero, 0)


def swiglu_local(rows, slots, free, tok_bm, tokt_bm, store, hgrad, interpret=False):
    row_blocks, tok_count, tile = tok_bm.shape
    tile_count = rows.shape[1]
    free_count = free.shape[1]
    smem = pl.BlockSpec(memory_space=pltpu.SMEM)
    vmem = pl.BlockSpec(memory_space=pltpu.VMEM)
    hbm = pl.BlockSpec(memory_space=pl.ANY)
    out_shape = (
        jax.ShapeDtypeStruct(hgrad.shape, jnp.bfloat16),
        jax.ShapeDtypeStruct((row_blocks, tile, tok_count), jnp.bfloat16),
        jax.ShapeDtypeStruct(store.shape, jnp.bfloat16),
    )
    return pl.pallas_call(
        _swiglu_kernel,
        out_shape=out_shape,
        in_specs=[smem, smem, smem, vmem, vmem, hbm, vmem],
        out_specs=(vmem, vmem, hbm),
        scratch_shapes=[pltpu.VMEM((row_blocks, tile, tok_count), jnp.float32),
                        pltpu.VMEM((2, tile_count, tile, tile), jnp.bfloat16),
                        pltpu.VMEM((2, tile_count, tile, tile), jnp.bfloat16),
                        pltpu.VMEM((tile_count // (hgrad.shape[1] // tile) * tile, tok_count), jnp.bfloat16),
                        pltpu.VMEM((tile, tile), jnp.bfloat16),
                        pltpu.SemaphoreType.DMA((2 * tile_count,)),
                        pltpu.SemaphoreType.DMA((2 * tile_count,)),
                        pltpu.SemaphoreType.DMA((2 * free_count,))],
        compiler_params=pltpu.CompilerParams(vmem_limit_bytes=100 * 1024 * 1024),
        interpret=interpret,
    )(rows, slots, free, tok_bm, tokt_bm, store, hgrad)


def free_slots(slots, slot_total):
    taken = jnp.zeros((slots.shape[0], slot_total), jnp.int32).at[
        jnp.arange(slots.shape[0])[:, None], slots].set(1)
    order = jnp.argsort(taken, axis=1, stable=True).astype(jnp.int32)
    return order[:, : slot_total - slots.shape[1]]


def body(tokens, hidden_grad, gate_tiles, up_tiles, tile_rows, tile_owner):
    tile_size = gate_tiles.shape[2]
    capacity = gate_tiles.shape[1]
    tensor_count = lax.axis_size("tensor")
    tok_copies = jnp.broadcast_to(tokens[None], (tensor_count,) + tokens.shape)
    gathered_tok = lax.all_to_all(tok_copies, "tensor", 0, 0, tiled=True).reshape(
        tensor_count * tokens.shape[0], tokens.shape[1]
    )
    tok_count, model_width = gathered_tok.shape
    row_blocks = model_width // tile_size
    tok_blocks = gathered_tok.reshape(tok_count, row_blocks, tile_size)
    tok_bm = tok_blocks.transpose(1, 0, 2)
    tokt_bm = tok_blocks.transpose(1, 2, 0)
    tile_count = tile_rows.shape[1] * tile_rows.shape[2]
    row_flat = tile_rows.reshape(2, tile_count)
    slot_stack = jnp.stack(
        [
            slot_index(tile_owner[0].reshape(-1), capacity),
            slot_index(tile_owner[1].reshape(-1), capacity),
        ],
        axis=0,
    )
    local_pair = jnp.stack([gate_tiles[0], up_tiles[0]], axis=1)
    store = lax.all_gather(local_pair, "dp", axis=0, tiled=True)
    free = free_slots(slot_stack, store.shape[0])
    hidden, tpart_t, grads = swiglu_local(
        row_flat, slot_stack, free, tok_bm, tokt_bm, store, hidden_grad
    )
    token_part = tpart_t.transpose(2, 0, 1).reshape(tok_count, model_width)
    part_rows = token_part.reshape(tensor_count, tok_count // tensor_count, model_width)
    part_recv = lax.all_to_all(part_rows, "tensor", 0, 0, tiled=True)
    token_grad = jnp.sum(part_recv.astype(jnp.float32), axis=0).astype(jnp.bfloat16)
    tile_sums = lax.psum_scatter(grads, "dp", scatter_dimension=0, tiled=True)
    gate_grad = tile_sums[:, 0][None]
    up_grad = tile_sums[:, 1][None]
    return (hidden, token_grad, gate_grad, up_grad)


def solution(mesh):
    placed = (
        P(("dp", "tensor"), None),
        P("dp", "tensor"),
        P("tensor", "dp", None, None),
        P("tensor", "dp", None, None),
        P(None, "tensor", None),
        P(None, "tensor", None),
    )
    return jax.shard_map(
        body,
        mesh=mesh,
        in_specs=placed,
        out_specs=(
            P("dp", "tensor"),
            P(("dp", "tensor"), None),
            P("tensor", "dp", None, None),
            P("tensor", "dp", None, None),
        ),
        check_vma=False,
    )
```

```python
import jax
import jax.numpy as jnp
from jax import lax
from jax.experimental import pallas as pl
from jax.experimental.pallas import tpu as pltpu
from jax.sharding import PartitionSpec as P


def slot_index(owner_ids, capacity):
    tile_total = owner_ids.shape[0]
    tile_order = jnp.arange(tile_total, dtype=jnp.int32)
    same_owner = (owner_ids[:, None] == owner_ids[None, :]) & (
        tile_order[None, :] < tile_order[:, None]
    )
    tile_ranks = jnp.sum(same_owner.astype(jnp.int32), axis=1)
    return owner_ids * capacity + tile_ranks


def _swiglu_kernel(rows_ref, slots_ref, free_ref, tok_ref, store_hbm, hgrad_ref,
                   hidden_ref, tpart_ref, grad_hbm, acc_ref, panel_ref, term_ref, picked_ref,
                   zero_ref, in_sem, out_sem, zero_sem):
    group_blocks = hgrad_ref.shape[1] // 128
    tile_count = rows_ref.shape[1]
    free_count = free_ref.shape[1]
    per_block = tile_count // group_blocks
    tile = panel_ref.shape[2]

    def tile_copy_in(m, i):
        s = slots_ref[m, i]
        return pltpu.make_async_copy(store_hbm.at[s, m], panel_ref.at[m, i],
                                     in_sem.at[m * tile_count + i])

    def tile_copy_out(m, i):
        s = slots_ref[m, i]
        return pltpu.make_async_copy(term_ref.at[m, i], grad_hbm.at[s, m],
                                     out_sem.at[m * tile_count + i])

    def zero_copy(m, j):
        u = free_ref[m, j]
        return pltpu.make_async_copy(zero_ref, grad_hbm.at[u, m], zero_sem.at[m * free_count + j])

    def start_in(i, carry):
        for m in range(2):
            tile_copy_in(m, i).start()
        return carry
    lax.fori_loop(0, tile_count, start_in, 0)
    zero_ref[...] = jnp.zeros(zero_ref.shape, zero_ref.dtype)

    def start_zero(j, carry):
        for m in range(2):
            zero_copy(m, j).start()
        return carry
    lax.fori_loop(0, free_count, start_zero, 0)
    acc_ref[...] = jnp.zeros(acc_ref.shape, jnp.float32)
    for f in range(group_blocks):
        for m in range(2):
            for k in range(per_block):
                r = rows_ref[m, f * per_block + k]
                picked_ref[m, :, k * tile:(k + 1) * tile] = tok_ref[r]

        def wait_in(k, carry, f=f):
            for m in range(2):
                tile_copy_in(m, f * per_block + k).wait()
            return carry
        lax.fori_loop(0, per_block, wait_in, 0)
        panels = [panel_ref[m, f * per_block:(f + 1) * per_block].reshape(per_block * tile, tile)
                  for m in range(2)]
        gate_pre, up_pre = [jnp.dot(picked_ref[m], panels[m], preferred_element_type=jnp.float32)
                            for m in range(2)]
        cols = slice(f * tile, (f + 1) * tile)
        hg = hgrad_ref[:, cols].astype(jnp.float32)
        sig = 1.0 / (1.0 + jnp.exp(-gate_pre))
        hidden_ref[:, cols] = (gate_pre * sig * up_pre).astype(hidden_ref.dtype)
        gate_delta = (hg * up_pre * sig * (1.0 + gate_pre * (1.0 - sig))).astype(jnp.bfloat16)
        up_delta = (hg * gate_pre * sig).astype(jnp.bfloat16)
        for m, delta in ((0, gate_delta), (1, up_delta)):
            delta_t = delta.astype(jnp.float32).T.astype(jnp.bfloat16)
            back = lax.dot_general(delta, panels[m], (((1,), (1,)), ((), ())),
                                   preferred_element_type=jnp.float32)
            term_t = jnp.dot(delta_t, picked_ref[m], preferred_element_type=jnp.float32)
            for k in range(per_block):
                i = f * per_block + k
                r = rows_ref[m, i]
                blk = slice(k * tile, (k + 1) * tile)
                acc_ref[r] = acc_ref[r] + back[:, blk]
                term_ref[m, i] = term_t[:, blk].astype(term_ref.dtype)
                tile_copy_out(m, i).start()
    tpart_ref[...] = acc_ref[...].astype(tpart_ref.dtype)

    def wait_out(i, carry):
        for m in range(2):
            tile_copy_out(m, i).wait()
        return carry
    lax.fori_loop(0, tile_count, wait_out, 0)

    def wait_zero(j, carry):
        for m in range(2):
            zero_copy(m, j).wait()
        return carry
    lax.fori_loop(0, free_count, wait_zero, 0)


def swiglu_local(rows, slots, free, tok_bm, store, hgrad, interpret=False):
    row_blocks, tok_count, tile = tok_bm.shape
    tile_count = rows.shape[1]
    free_count = free.shape[1]
    per_block = tile_count // (hgrad.shape[1] // tile)
    smem = pl.BlockSpec(memory_space=pltpu.SMEM)
    vmem = pl.BlockSpec(memory_space=pltpu.VMEM)
    hbm = pl.BlockSpec(memory_space=pl.ANY)
    out_shape = (
        jax.ShapeDtypeStruct(hgrad.shape, jnp.bfloat16),
        jax.ShapeDtypeStruct((row_blocks, tok_count, tile), jnp.bfloat16),
        jax.ShapeDtypeStruct(store.shape, jnp.bfloat16),
    )
    return pl.pallas_call(
        _swiglu_kernel,
        out_shape=out_shape,
        in_specs=[smem, smem, smem, vmem, hbm, vmem],
        out_specs=(vmem, vmem, hbm),
        scratch_shapes=[pltpu.VMEM((row_blocks, tok_count, tile), jnp.float32),
                        pltpu.VMEM((2, tile_count, tile, tile), jnp.bfloat16),
                        pltpu.VMEM((2, tile_count, tile, tile), jnp.bfloat16),
                        pltpu.VMEM((2, tok_count, per_block * tile), jnp.bfloat16),
                        pltpu.VMEM((tile, tile), jnp.bfloat16),
                        pltpu.SemaphoreType.DMA((2 * tile_count,)),
                        pltpu.SemaphoreType.DMA((2 * tile_count,)),
                        pltpu.SemaphoreType.DMA((2 * free_count,))],
        compiler_params=pltpu.CompilerParams(vmem_limit_bytes=100 * 1024 * 1024),
        interpret=interpret,
    )(rows, slots, free, tok_bm, store, hgrad)


def free_slots(slots, slot_total):
    taken = jnp.zeros((slots.shape[0], slot_total), jnp.int32).at[
        jnp.arange(slots.shape[0])[:, None], slots].set(1)
    order = jnp.argsort(taken, axis=1, stable=True).astype(jnp.int32)
    return order[:, : slot_total - slots.shape[1]]


def body(tokens, hidden_grad, gate_tiles, up_tiles, tile_rows, tile_owner):
    tile_size = gate_tiles.shape[2]
    capacity = gate_tiles.shape[1]
    tensor_count = lax.axis_size("tensor")
    tok_copies = jnp.broadcast_to(tokens[None], (tensor_count,) + tokens.shape)
    gathered_tok = lax.all_to_all(tok_copies, "tensor", 0, 0, tiled=True).reshape(
        tensor_count * tokens.shape[0], tokens.shape[1]
    )
    tok_count, model_width = gathered_tok.shape
    row_blocks = model_width // tile_size
    tok_blocks = gathered_tok.reshape(tok_count, row_blocks, tile_size)
    tok_bm = tok_blocks.transpose(1, 0, 2)
    tile_count = tile_rows.shape[1] * tile_rows.shape[2]
    row_flat = tile_rows.reshape(2, tile_count)
    slot_stack = jnp.stack(
        [
            slot_index(tile_owner[0].reshape(-1), capacity),
            slot_index(tile_owner[1].reshape(-1), capacity),
        ],
        axis=0,
    )
    local_pair = jnp.stack([gate_tiles[0], up_tiles[0]], axis=1)
    store = lax.all_gather(local_pair, "dp", axis=0, tiled=True)
    free = free_slots(slot_stack, store.shape[0])
    hidden, tpart_bm, grads_t = swiglu_local(
        row_flat, slot_stack, free, tok_bm, store, hidden_grad
    )
    token_part = tpart_bm.transpose(1, 0, 2).reshape(tok_count, model_width)
    part_rows = token_part.reshape(tensor_count, tok_count // tensor_count, model_width)
    part_recv = lax.all_to_all(part_rows, "tensor", 0, 0, tiled=True)
    token_grad = jnp.sum(part_recv.astype(jnp.float32), axis=0).astype(jnp.bfloat16)
    tile_sums = lax.psum_scatter(grads_t, "dp", scatter_dimension=0, tiled=True).transpose(
        0, 1, 3, 2
    )
    gate_grad = tile_sums[:, 0][None]
    up_grad = tile_sums[:, 1][None]
    return (hidden, token_grad, gate_grad, up_grad)


def solution(mesh):
    placed = (
        P(("dp", "tensor"), None),
        P("dp", "tensor"),
        P("tensor", "dp", None, None),
        P("tensor", "dp", None, None),
        P(None, "tensor", None),
        P(None, "tensor", None),
    )
    return jax.shard_map(
        body,
        mesh=mesh,
        in_specs=placed,
        out_specs=(
            P("dp", "tensor"),
            P(("dp", "tensor"), None),
            P("tensor", "dp", None, None),
            P("tensor", "dp", None, None),
        ),
        check_vma=False,
    )
```

```python
import jax
import jax.numpy as jnp
from jax import lax
from jax.experimental import pallas as pl
from jax.experimental.pallas import tpu as pltpu
from jax.sharding import PartitionSpec as P


def slot_index(owner_ids, capacity):
    tile_total = owner_ids.shape[0]
    tile_order = jnp.arange(tile_total, dtype=jnp.int32)
    same_owner = (owner_ids[:, None] == owner_ids[None, :]) & (
        tile_order[None, :] < tile_order[:, None]
    )
    tile_ranks = jnp.sum(same_owner.astype(jnp.int32), axis=1)
    return owner_ids * capacity + tile_ranks


def _swiglu_kernel(rows_ref, slots_ref, tok_ref, store_ref, hgrad_ref,
                   hidden_ref, tpart_ref, grad_ref, acc_ref, panel_ref, picked_ref):
    group_blocks = hgrad_ref.shape[1] // 128
    tile_count = rows_ref.shape[1]
    per_block = tile_count // group_blocks
    tile = store_ref.shape[2]
    acc_ref[...] = jnp.zeros(acc_ref.shape, jnp.float32)
    grad_ref[...] = jnp.zeros(grad_ref.shape, grad_ref.dtype)
    for f in range(group_blocks):
        for m in range(2):
            for k in range(per_block):
                i = f * per_block + k
                r = rows_ref[m, i]
                s = slots_ref[m, i]
                blk = slice(k * tile, (k + 1) * tile)
                picked_ref[m, :, blk] = tok_ref[r]
                panel_ref[m, blk, :] = store_ref[s, m]
        gate_pre, up_pre = [jnp.dot(picked_ref[m], panel_ref[m], preferred_element_type=jnp.float32)
                            for m in range(2)]
        cols = slice(f * tile, (f + 1) * tile)
        hg = hgrad_ref[:, cols].astype(jnp.float32)
        sig = 1.0 / (1.0 + jnp.exp(-gate_pre))
        hidden_ref[:, cols] = (gate_pre * sig * up_pre).astype(hidden_ref.dtype)
        gate_delta = (hg * up_pre * sig * (1.0 + gate_pre * (1.0 - sig))).astype(jnp.bfloat16)
        up_delta = (hg * gate_pre * sig).astype(jnp.bfloat16)
        for m, delta in ((0, gate_delta), (1, up_delta)):
            delta_t = delta.astype(jnp.float32).T.astype(jnp.bfloat16)
            back = lax.dot_general(delta, panel_ref[m], (((1,), (1,)), ((), ())),
                                   preferred_element_type=jnp.float32)
            term_t = jnp.dot(delta_t, picked_ref[m], preferred_element_type=jnp.float32)
            for k in range(per_block):
                i = f * per_block + k
                r = rows_ref[m, i]
                s = slots_ref[m, i]
                blk = slice(k * tile, (k + 1) * tile)
                acc_ref[r] = acc_ref[r] + back[:, blk]
                grad_ref[s, m] = term_t[:, blk].astype(grad_ref.dtype)
    tpart_ref[...] = acc_ref[...].astype(tpart_ref.dtype)


def swiglu_local(rows, slots, tok_bm, store, hgrad, interpret=False):
    row_blocks, tok_count, tile = tok_bm.shape
    tile_count = rows.shape[1]
    per_block = tile_count // (hgrad.shape[1] // tile)
    smem = pl.BlockSpec(memory_space=pltpu.SMEM)
    vmem = pl.BlockSpec(memory_space=pltpu.VMEM)
    out_shape = (
        jax.ShapeDtypeStruct(hgrad.shape, jnp.bfloat16),
        jax.ShapeDtypeStruct((row_blocks, tok_count, tile), jnp.bfloat16),
        jax.ShapeDtypeStruct(store.shape, jnp.bfloat16),
    )
    return pl.pallas_call(
        _swiglu_kernel,
        out_shape=out_shape,
        in_specs=[smem, smem, vmem, vmem, vmem],
        out_specs=(vmem, vmem, vmem),
        scratch_shapes=[pltpu.VMEM((row_blocks, tok_count, tile), jnp.float32),
                        pltpu.VMEM((2, per_block * tile, tile), jnp.bfloat16),
                        pltpu.VMEM((2, tok_count, per_block * tile), jnp.bfloat16)],
        compiler_params=pltpu.CompilerParams(vmem_limit_bytes=100 * 1024 * 1024),
        interpret=interpret,
    )(rows, slots, tok_bm, store, hgrad)


def body(tokens, hidden_grad, gate_tiles, up_tiles, tile_rows, tile_owner):
    tile_size = gate_tiles.shape[2]
    capacity = gate_tiles.shape[1]
    tensor_count = lax.axis_size("tensor")
    tok_copies = jnp.broadcast_to(tokens[None], (tensor_count,) + tokens.shape)
    gathered_tok = lax.all_to_all(tok_copies, "tensor", 0, 0, tiled=True).reshape(
        tensor_count * tokens.shape[0], tokens.shape[1]
    )
    tok_count, model_width = gathered_tok.shape
    row_blocks = model_width // tile_size
    tok_blocks = gathered_tok.reshape(tok_count, row_blocks, tile_size)
    tok_bm = tok_blocks.transpose(1, 0, 2)
    tile_count = tile_rows.shape[1] * tile_rows.shape[2]
    row_flat = tile_rows.reshape(2, tile_count)
    slot_stack = jnp.stack(
        [
            slot_index(tile_owner[0].reshape(-1), capacity),
            slot_index(tile_owner[1].reshape(-1), capacity),
        ],
        axis=0,
    )
    local_pair = jnp.stack([gate_tiles[0], up_tiles[0]], axis=1)
    store = lax.all_gather(local_pair, "dp", axis=0, tiled=True)
    hidden, tpart_bm, grads_t = swiglu_local(row_flat, slot_stack, tok_bm, store, hidden_grad)
    token_part = tpart_bm.transpose(1, 0, 2).reshape(tok_count, model_width)
    part_rows = token_part.reshape(tensor_count, tok_count // tensor_count, model_width)
    part_recv = lax.all_to_all(part_rows, "tensor", 0, 0, tiled=True)
    token_grad = jnp.sum(part_recv.astype(jnp.float32), axis=0).astype(jnp.bfloat16)
    tile_sums = lax.psum_scatter(grads_t, "dp", scatter_dimension=0, tiled=True).transpose(
        0, 1, 3, 2
    )
    gate_grad = tile_sums[:, 0][None]
    up_grad = tile_sums[:, 1][None]
    return (hidden, token_grad, gate_grad, up_grad)


def solution(mesh):
    placed = (
        P(("dp", "tensor"), None),
        P("dp", "tensor"),
        P("tensor", "dp", None, None),
        P("tensor", "dp", None, None),
        P(None, "tensor", None),
        P(None, "tensor", None),
    )
    return jax.shard_map(
        body,
        mesh=mesh,
        in_specs=placed,
        out_specs=(
            P("dp", "tensor"),
            P(("dp", "tensor"), None),
            P("tensor", "dp", None, None),
            P("tensor", "dp", None, None),
        ),
        check_vma=False,
    )
```

```python
import jax
import jax.numpy as jnp
from jax import lax
from jax.experimental import pallas as pl
from jax.experimental.pallas import tpu as pltpu
from jax.sharding import PartitionSpec as P


def slot_index(owner_ids, capacity):
    tile_total = owner_ids.shape[0]
    tile_order = jnp.arange(tile_total, dtype=jnp.int32)
    same_owner = (owner_ids[:, None] == owner_ids[None, :]) & (
        tile_order[None, :] < tile_order[:, None]
    )
    tile_ranks = jnp.sum(same_owner.astype(jnp.int32), axis=1)
    return owner_ids * capacity + tile_ranks


def _swiglu_kernel(rows_ref, slots_ref, tok_ref, store_hbm, hgrad_ref,
                   hidden_ref, tpart_ref, grad_ref, acc_ref, panel_ref, picked_ref,
                   store_ref, store_sem):
    group_blocks = hgrad_ref.shape[1] // 128
    tile_count = rows_ref.shape[1]
    per_block = tile_count // group_blocks
    tile = store_ref.shape[2]
    store_copy = pltpu.make_async_copy(store_hbm, store_ref, store_sem)
    store_copy.start()
    acc_ref[...] = jnp.zeros(acc_ref.shape, jnp.float32)
    grad_ref[...] = jnp.zeros(grad_ref.shape, grad_ref.dtype)
    store_copy.wait()
    for f in range(group_blocks):
        for m in range(2):
            for k in range(per_block):
                i = f * per_block + k
                r = rows_ref[m, i]
                s = slots_ref[m, i]
                blk = slice(k * tile, (k + 1) * tile)
                picked_ref[m, :, blk] = tok_ref[r]
                panel_ref[m, blk, :] = store_ref[s, m]
        gate_pre, up_pre = [jnp.dot(picked_ref[m], panel_ref[m], preferred_element_type=jnp.float32)
                            for m in range(2)]
        cols = slice(f * tile, (f + 1) * tile)
        hg = hgrad_ref[:, cols].astype(jnp.float32)
        sig = 1.0 / (1.0 + jnp.exp(-gate_pre))
        hidden_ref[:, cols] = (gate_pre * sig * up_pre).astype(hidden_ref.dtype)
        gate_delta = (hg * up_pre * sig * (1.0 + gate_pre * (1.0 - sig))).astype(jnp.bfloat16)
        up_delta = (hg * gate_pre * sig).astype(jnp.bfloat16)
        for m, delta in ((0, gate_delta), (1, up_delta)):
            delta_t = delta.astype(jnp.float32).T.astype(jnp.bfloat16)
            back = lax.dot_general(delta, panel_ref[m], (((1,), (1,)), ((), ())),
                                   preferred_element_type=jnp.float32)
            term_t = jnp.dot(delta_t, picked_ref[m], preferred_element_type=jnp.float32)
            for k in range(per_block):
                i = f * per_block + k
                r = rows_ref[m, i]
                s = slots_ref[m, i]
                blk = slice(k * tile, (k + 1) * tile)
                acc_ref[r] = acc_ref[r] + back[:, blk]
                grad_ref[s, m] = term_t[:, blk].astype(grad_ref.dtype)
    tpart_ref[...] = acc_ref[...].astype(tpart_ref.dtype)


def swiglu_local(rows, slots, tok_bm, store, hgrad, interpret=False):
    row_blocks, tok_count, tile = tok_bm.shape
    tile_count = rows.shape[1]
    per_block = tile_count // (hgrad.shape[1] // tile)
    smem = pl.BlockSpec(memory_space=pltpu.SMEM)
    vmem = pl.BlockSpec(memory_space=pltpu.VMEM)
    out_shape = (
        jax.ShapeDtypeStruct(hgrad.shape, jnp.bfloat16),
        jax.ShapeDtypeStruct((row_blocks, tok_count, tile), jnp.bfloat16),
        jax.ShapeDtypeStruct(store.shape, jnp.bfloat16),
    )
    return pl.pallas_call(
        _swiglu_kernel,
        out_shape=out_shape,
        in_specs=[smem, smem, vmem, pl.BlockSpec(memory_space=pl.ANY), vmem],
        out_specs=(vmem, vmem, vmem),
        scratch_shapes=[pltpu.VMEM((row_blocks, tok_count, tile), jnp.float32),
                        pltpu.VMEM((2, per_block * tile, tile), jnp.bfloat16),
                        pltpu.VMEM((2, tok_count, per_block * tile), jnp.bfloat16),
                        pltpu.VMEM(store.shape, jnp.bfloat16),
                        pltpu.SemaphoreType.DMA(())],
        compiler_params=pltpu.CompilerParams(vmem_limit_bytes=100 * 1024 * 1024),
        interpret=interpret,
    )(rows, slots, tok_bm, store, hgrad)


def body(tokens, hidden_grad, gate_tiles, up_tiles, tile_rows, tile_owner):
    tile_size = gate_tiles.shape[2]
    capacity = gate_tiles.shape[1]
    tensor_count = lax.axis_size("tensor")
    tok_copies = jnp.broadcast_to(tokens[None], (tensor_count,) + tokens.shape)
    gathered_tok = lax.all_to_all(tok_copies, "tensor", 0, 0, tiled=True).reshape(
        tensor_count * tokens.shape[0], tokens.shape[1]
    )
    tok_count, model_width = gathered_tok.shape
    row_blocks = model_width // tile_size
    tok_blocks = gathered_tok.reshape(tok_count, row_blocks, tile_size)
    tok_bm = tok_blocks.transpose(1, 0, 2)
    tile_count = tile_rows.shape[1] * tile_rows.shape[2]
    row_flat = tile_rows.reshape(2, tile_count)
    slot_stack = jnp.stack(
        [
            slot_index(tile_owner[0].reshape(-1), capacity),
            slot_index(tile_owner[1].reshape(-1), capacity),
        ],
        axis=0,
    )
    local_pair = jnp.stack([gate_tiles[0], up_tiles[0]], axis=1)
    store = lax.all_gather(local_pair, "dp", axis=0, tiled=True)
    hidden, tpart_bm, grads_t = swiglu_local(row_flat, slot_stack, tok_bm, store, hidden_grad)
    token_part = tpart_bm.transpose(1, 0, 2).reshape(tok_count, model_width)
    part_rows = token_part.reshape(tensor_count, tok_count // tensor_count, model_width)
    part_recv = lax.all_to_all(part_rows, "tensor", 0, 0, tiled=True)
    token_grad = jnp.sum(part_recv.astype(jnp.float32), axis=0).astype(jnp.bfloat16)
    tile_sums = lax.psum_scatter(grads_t, "dp", scatter_dimension=0, tiled=True).transpose(
        0, 1, 3, 2
    )
    gate_grad = tile_sums[:, 0][None]
    up_grad = tile_sums[:, 1][None]
    return (hidden, token_grad, gate_grad, up_grad)


def solution(mesh):
    placed = (
        P(("dp", "tensor"), None),
        P("dp", "tensor"),
        P("tensor", "dp", None, None),
        P("tensor", "dp", None, None),
        P(None, "tensor", None),
        P(None, "tensor", None),
    )
    return jax.shard_map(
        body,
        mesh=mesh,
        in_specs=placed,
        out_specs=(
            P("dp", "tensor"),
            P(("dp", "tensor"), None),
            P("tensor", "dp", None, None),
            P("tensor", "dp", None, None),
        ),
        check_vma=False,
    )
```

```python
import jax
import jax.numpy as jnp
from jax import lax
from jax.experimental import pallas as pl
from jax.experimental.pallas import tpu as pltpu
from jax.sharding import PartitionSpec as P


def slot_index(owner_ids, capacity):
    tile_total = owner_ids.shape[0]
    tile_order = jnp.arange(tile_total, dtype=jnp.int32)
    same_owner = (owner_ids[:, None] == owner_ids[None, :]) & (
        tile_order[None, :] < tile_order[:, None]
    )
    tile_ranks = jnp.sum(same_owner.astype(jnp.int32), axis=1)
    return owner_ids * capacity + tile_ranks


def _swiglu_kernel(rows_ref, slots_ref, near_ref, far_ref, tok_ref, store_hbm, rest_ref,
                   hgrad_ref, hidden_ref, tpart_ref, grad_ref, acc_ref, panel_ref, picked_ref,
                   store_ref, store_sem):
    group_blocks = hgrad_ref.shape[1] // 128
    tile_count = rows_ref.shape[1]
    per_block = tile_count // group_blocks
    tile = store_ref.shape[2]
    store_copy = pltpu.make_async_copy(store_hbm, store_ref, store_sem)
    store_copy.start()
    acc_ref[...] = jnp.zeros(acc_ref.shape, jnp.float32)
    grad_ref[...] = jnp.zeros(grad_ref.shape, grad_ref.dtype)
    store_copy.wait()
    for f in range(group_blocks):
        for m in range(2):
            for k in range(per_block):
                i = f * per_block + k
                r = rows_ref[m, i]
                blk = slice(k * tile, (k + 1) * tile)
                near = near_ref[m, i]
                far = far_ref[m, i]
                picked_ref[m, :, blk] = tok_ref[r]

                @pl.when(far < 0)
                def _(m=m, blk=blk, near=near):
                    panel_ref[m, blk, :] = store_ref[near, m]

                @pl.when(far >= 0)
                def _(m=m, blk=blk, far=far):
                    panel_ref[m, blk, :] = rest_ref[far, m]
        gate_pre, up_pre = [jnp.dot(picked_ref[m], panel_ref[m], preferred_element_type=jnp.float32)
                            for m in range(2)]
        cols = slice(f * tile, (f + 1) * tile)
        hg = hgrad_ref[:, cols].astype(jnp.float32)
        sig = 1.0 / (1.0 + jnp.exp(-gate_pre))
        hidden_ref[:, cols] = (gate_pre * sig * up_pre).astype(hidden_ref.dtype)
        gate_delta = (hg * up_pre * sig * (1.0 + gate_pre * (1.0 - sig))).astype(jnp.bfloat16)
        up_delta = (hg * gate_pre * sig).astype(jnp.bfloat16)
        for m, delta in ((0, gate_delta), (1, up_delta)):
            delta_t = delta.astype(jnp.float32).T.astype(jnp.bfloat16)
            back = lax.dot_general(delta, panel_ref[m], (((1,), (1,)), ((), ())),
                                   preferred_element_type=jnp.float32)
            term_t = jnp.dot(delta_t, picked_ref[m], preferred_element_type=jnp.float32)
            for k in range(per_block):
                i = f * per_block + k
                r = rows_ref[m, i]
                s = slots_ref[m, i]
                blk = slice(k * tile, (k + 1) * tile)
                acc_ref[r] = acc_ref[r] + back[:, blk]
                grad_ref[s, m] = term_t[:, blk].astype(grad_ref.dtype)
    tpart_ref[...] = acc_ref[...].astype(tpart_ref.dtype)


def swiglu_local(rows, slots, near, far, tok_bm, store, rest, hgrad, interpret=False):
    row_blocks, tok_count, tile = tok_bm.shape
    slot_total = store.shape[0] + rest.shape[0]
    tile_count = rows.shape[1]
    per_block = tile_count // (hgrad.shape[1] // tile)
    smem = pl.BlockSpec(memory_space=pltpu.SMEM)
    vmem = pl.BlockSpec(memory_space=pltpu.VMEM)
    out_shape = (
        jax.ShapeDtypeStruct(hgrad.shape, jnp.bfloat16),
        jax.ShapeDtypeStruct((row_blocks, tok_count, tile), jnp.bfloat16),
        jax.ShapeDtypeStruct((slot_total,) + store.shape[1:], jnp.bfloat16),
    )
    return pl.pallas_call(
        _swiglu_kernel,
        out_shape=out_shape,
        in_specs=[smem, smem, smem, smem, vmem, pl.BlockSpec(memory_space=pl.ANY), vmem, vmem],
        out_specs=(vmem, vmem, vmem),
        scratch_shapes=[pltpu.VMEM((row_blocks, tok_count, tile), jnp.float32),
                        pltpu.VMEM((2, per_block * tile, tile), jnp.bfloat16),
                        pltpu.VMEM((2, tok_count, per_block * tile), jnp.bfloat16),
                        pltpu.VMEM(store.shape, jnp.bfloat16),
                        pltpu.SemaphoreType.DMA(())],
        compiler_params=pltpu.CompilerParams(vmem_limit_bytes=100 * 1024 * 1024),
        interpret=interpret,
    )(rows, slots, near, far, tok_bm, store, rest, hgrad)


def body(tokens, hidden_grad, gate_tiles, up_tiles, tile_rows, tile_owner):
    tile_size = gate_tiles.shape[2]
    capacity = gate_tiles.shape[1]
    tensor_count = lax.axis_size("tensor")
    tok_copies = jnp.broadcast_to(tokens[None], (tensor_count,) + tokens.shape)
    gathered_tok = lax.all_to_all(tok_copies, "tensor", 0, 0, tiled=True).reshape(
        tensor_count * tokens.shape[0], tokens.shape[1]
    )
    tok_count, model_width = gathered_tok.shape
    row_blocks = model_width // tile_size
    tok_blocks = gathered_tok.reshape(tok_count, row_blocks, tile_size)
    tok_bm = tok_blocks.transpose(1, 0, 2)
    tile_count = tile_rows.shape[1] * tile_rows.shape[2]
    row_flat = tile_rows.reshape(2, tile_count)
    slot_stack = jnp.stack(
        [
            slot_index(tile_owner[0].reshape(-1), capacity),
            slot_index(tile_owner[1].reshape(-1), capacity),
        ],
        axis=0,
    )
    local_pair = jnp.stack([gate_tiles[0], up_tiles[0]], axis=1)
    owner_count = lax.axis_size("dp")
    near_count = capacity - capacity // 4
    far_count = capacity - near_count
    store = lax.all_gather(local_pair[:near_count], "dp", axis=0, tiled=True)
    far_copies = jnp.broadcast_to(
        local_pair[near_count:][None], (owner_count,) + local_pair[near_count:].shape
    )
    rest = lax.all_to_all(far_copies, "dp", 0, 0, tiled=True).reshape(
        (owner_count * far_count,) + local_pair.shape[1:]
    )
    slot_owner = slot_stack // capacity
    slot_rank = slot_stack % capacity
    near = slot_owner * near_count + jnp.minimum(slot_rank, near_count - 1)
    far = jnp.where(slot_rank >= near_count, slot_owner * far_count + slot_rank - near_count, -1)
    hidden, tpart_bm, grads_t = swiglu_local(
        row_flat, slot_stack, near, far, tok_bm, store, rest, hidden_grad
    )
    token_part = tpart_bm.transpose(1, 0, 2).reshape(tok_count, model_width)
    part_rows = token_part.reshape(tensor_count, tok_count // tensor_count, model_width)
    part_recv = lax.all_to_all(part_rows, "tensor", 0, 0, tiled=True)
    token_grad = jnp.sum(part_recv.astype(jnp.float32), axis=0).astype(jnp.bfloat16)
    tile_sums = lax.psum_scatter(grads_t, "dp", scatter_dimension=0, tiled=True).transpose(
        0, 1, 3, 2
    )
    gate_grad = tile_sums[:, 0][None]
    up_grad = tile_sums[:, 1][None]
    return (hidden, token_grad, gate_grad, up_grad)


def solution(mesh):
    placed = (
        P(("dp", "tensor"), None),
        P("dp", "tensor"),
        P("tensor", "dp", None, None),
        P("tensor", "dp", None, None),
        P(None, "tensor", None),
        P(None, "tensor", None),
    )
    return jax.shard_map(
        body,
        mesh=mesh,
        in_specs=placed,
        out_specs=(
            P("dp", "tensor"),
            P(("dp", "tensor"), None),
            P("tensor", "dp", None, None),
            P("tensor", "dp", None, None),
        ),
        check_vma=False,
    )
```
